512 devices in a mesh: seq: 32 (over z, x_hi), fsdp: 16 (over y, x_lo, core).
Axes of the slice: x: 4 (x_hi: 2, x_lo: 2; x = x_hi * 2 + x_lo), y: 4, z: 16, core: 2. Of those that a mesh axis runs over, the one named last changes fastest.
Arguments:
- inputs: bfloat16 [5376, 65536], P('fsdp', 'seq'), may hold values from -6 to 6
- value_weight: bfloat16 [5376, 1024], P('fsdp'), may hold values from -0.078125 to 0.078125
- threshold: float32 [1024], replicated, may hold values from 0.004 to 0.03
- queries: bfloat16 [65536, 2048], P(('seq', 'fsdp')), may hold values from -180 to 180
- keys: bfloat16 [65536, 1024], P(('seq', 'fsdp')), may hold values from -6 to 6
- out_grad: bfloat16 [65536, 2048], P(('seq', 'fsdp')), may hold values from -0.59765625 to 0.59765625
Outputs:
- grad_weight: bfloat16 [5376, 1024], P('fsdp')
- grad_logit: float32 [1024], replicated
The draws below stay inside these ranges and needn't reach their ends.
All inputs are finite; a program needn't handle non-finite values.
Results may differ from the reference program's by a relative error of at most 0.0058.
Values may be sent and summed in bfloat16 or wider, within the bound.
No kernel may reach another device: no remote copies, remote signals or barrier semaphores. Data moves between devices by JAX's collectives and lax.ppermute only.
A program may use at most 64 MiB of HBM per device.

```python
import math
import jax
import jax.numpy as jnp
from jax import lax

D = 5376
HEAD = 128
Q_HEADS = 16
KV_HEADS = 8
WINDOW = 1024
TOK_DEV = 128
Q_WIDTH = 2048
KV_WIDTH = 1024
TOKENS = 65536


def shared_parts(key):
    base = jax.random.truncated_normal(jax.random.fold_in(key, 11), -6.0, 6.0, (TOKENS, KV_WIDTH), jnp.float32)
    return base


def draw_keys(key, part):
    base = shared_parts(key)
    return base.astype(jnp.bfloat16)


def draw_queries(key, part):
    drawn = jax.random.truncated_normal(jax.random.fold_in(key, 21), -6.0, 6.0, (TOKENS, Q_WIDTH), jnp.float32)
    return drawn.astype(jnp.bfloat16)


def block_scale(stream_key, extent, shards, low, high):
    loudness, own = 1.0, jax.random.fold_in(stream_key, 6)
    for dim, parts in shards:
        heights = jnp.exp(jax.random.uniform(jax.random.fold_in(own, dim), (parts,), jnp.float32, low / len(shards), high / len(shards)))
        loudness = loudness * jnp.repeat(heights, extent[dim] // parts).reshape([-1 if axis == dim else 1 for axis in range(len(extent))])
    return loudness


def scatter_about(key, extent, scale, reach, pieces=(), held_as=jnp.bfloat16):
    factor_of = block_scale(key, extent, pieces, -0.22, 0.18) if pieces else 1.0
    drawn = jax.random.normal(key, extent, jnp.float32) * scale * factor_of
    return jnp.minimum(jnp.maximum(drawn, -reach), reach).astype(held_as)


def setup_inputs(seed: int = 0) -> dict:
    arg_keys = jax.random.split(jax.random.key(seed), 7)
    return {
        "inputs": scatter_about(arg_keys[0], (D, TOKENS), 1.0, 6.0, ((0, 16), (1, 32))),
        "value_weight": scatter_about(arg_keys[1], (D, KV_WIDTH), D ** -0.5, 0.078125, ((0, 16),)),
        "threshold": jnp.clip(jnp.exp(jax.random.uniform(arg_keys[2], (KV_WIDTH,), jnp.float32, math.log(0.004), math.log(0.03))), 0.004, 0.03),
        "queries": draw_queries(jax.random.fold_in(arg_keys[6], 71), 0),
        "keys": draw_keys(jax.random.fold_in(arg_keys[6], 71), 0),
        "out_grad": scatter_about(arg_keys[5], (TOKENS, Q_WIDTH), 0.1, 0.59765625, ((0, 512),)),
    }


pre_scale = 168.0 ** -0.5
masked_score = -1e30


def reference(inputs, value_weight, threshold, queries, keys, out_grad):
    block_count = TOKENS // TOK_DEV
    hop_count = WINDOW // TOK_DEV
    span_keys = (hop_count + 1) * TOK_DEV
    head_ratio = Q_HEADS // KV_HEADS
    padded_keys = jnp.concatenate([jnp.zeros((hop_count * TOK_DEV, KV_WIDTH), keys.dtype), keys], axis=0)
    start_acc = jnp.zeros(((block_count + hop_count) * TOK_DEV, KV_WIDTH), jnp.float32)

    def one_block(accum, block_idx):
        first = (block_idx * TOK_DEV).astype(jnp.int32)
        q_rows = lax.dynamic_slice_in_dim(queries, first, TOK_DEV, 0).reshape(TOK_DEV, KV_HEADS, head_ratio, HEAD)
        d_rows = lax.dynamic_slice_in_dim(out_grad, first, TOK_DEV, 0).reshape(TOK_DEV, KV_HEADS, head_ratio, HEAD)
        k_rows = lax.dynamic_slice_in_dim(padded_keys, first, span_keys, 0).reshape(span_keys, KV_HEADS, HEAD)
        query_pos = first + jnp.arange(TOK_DEV, dtype=jnp.int32)
        key_pos = first - hop_count * TOK_DEV + jnp.arange(span_keys, dtype=jnp.int32)
        offset = query_pos[:, None] - key_pos[None, :]
        visible = (offset >= 0) & (offset < WINDOW) & (key_pos >= 0)[None, :]
        scores = jnp.einsum('qgrd,kgd->grqk', q_rows.astype(jnp.float32), k_rows.astype(jnp.float32)) * pre_scale
        scores = jnp.where(visible, scores, masked_score)
        row_max = jnp.max(scores, axis=-1, keepdims=True)
        weights = jnp.exp(scores - row_max)
        probabilities = (weights / jnp.sum(weights, axis=-1, keepdims=True)).astype(jnp.bfloat16)
        value_part = jnp.einsum('grqk,qgrd->kgd', probabilities.astype(jnp.float32), d_rows.astype(jnp.float32))
        value_part = value_part.reshape(span_keys, KV_WIDTH)
        current = lax.dynamic_slice_in_dim(accum, first, span_keys, 0)
        accum = lax.dynamic_update_slice_in_dim(accum, current + value_part, first, 0)
        return accum, None

    accum, _ = lax.scan(one_block, start_acc, jnp.arange(block_count, dtype=jnp.int32))
    value_grad = accum[hop_count * TOK_DEV:].astype(jnp.bfloat16)
    dense_grad = jnp.dot(inputs, value_grad, preferred_element_type=jnp.float32)
    weight_full = value_weight.astype(jnp.float32)
    kept_mask = jnp.abs(weight_full) > threshold[None, :]
    grad_weight = jnp.where(kept_mask, dense_grad, 0.0).astype(jnp.bfloat16)
    signed = jnp.where(kept_mask, jnp.sign(weight_full), 0.0)
    grad_logit = -jnp.sum(dense_grad * signed, axis=0) * threshold * (1.0 - threshold)
    return grad_weight, grad_logit
```

```python
import math

import jax
import jax.numpy as jnp
from jax import lax
from jax.sharding import Mesh
from jax.sharding import PartitionSpec as P

HEAD = 128
Q_HEADS = 16
KV_HEADS = 8
WINDOW = 1024
TOK_DEV = 128


pre_scale = 168.0 ** (-0.5)
masked_score = -1e30

SEQ = ("z", "xh")
FSDP = ("y", "xl", "c")
ALL = SEQ + FSDP


def passed_along(value, axis, count, steps):
    first, last = (max(0, -steps), min(count, count - steps))
    return lax.ppermute(value, axis, [(source, source + steps) for source in range(first, last)])


def make_local(sizes):
    n_all = math.prod(sizes[a] for a in ALL)
    n_seq = math.prod(sizes[a] for a in SEQ)
    n_fsdp = math.prod(sizes[a] for a in FSDP)

    def local(inputs, value_weight, threshold, queries, keys, out_grad):
        tok_rows = queries.shape[0]
        hop_count = WINDOW // TOK_DEV
        span_keys = (hop_count + 1) * tok_rows
        head_ratio = Q_HEADS // KV_HEADS
        kv_pair = 2
        group_count = KV_HEADS // kv_pair
        position = lax.axis_index(ALL)
        earlier = [passed_along(keys, ALL, n_all, distance) for distance in range(hop_count, 0, -1)]
        key_rows = jnp.concatenate(earlier + [keys], axis=0)
        query_pos = position * tok_rows + jnp.arange(tok_rows, dtype=jnp.int32)
        key_pos = (position - hop_count) * tok_rows + jnp.arange(span_keys, dtype=jnp.int32)
        offset = query_pos[:, None] - key_pos[None, :]
        visible = (offset >= 0) & (offset < WINDOW) & (key_pos >= 0)[None, :]
        q_span = kv_pair * head_ratio * HEAD
        k_span = kv_pair * HEAD

        def group_step(group_index, running):
            q_cols = lax.dynamic_slice_in_dim(queries, group_index * q_span, q_span, 1).reshape(
                tok_rows, kv_pair, head_ratio, HEAD
            )
            d_cols = lax.dynamic_slice_in_dim(out_grad, group_index * q_span, q_span, 1).reshape(
                tok_rows, kv_pair, head_ratio, HEAD
            )
            k_cols = lax.dynamic_slice_in_dim(key_rows, group_index * k_span, k_span, 1).reshape(
                span_keys, kv_pair, HEAD
            )
            scores = (
                jnp.einsum("qgrd,kgd->grqk", q_cols, k_cols, preferred_element_type=jnp.float32)
                * pre_scale
            )
            scores = jnp.where(visible, scores, masked_score)
            row_max = jnp.max(scores, axis=-1, keepdims=True)
            weights = jnp.exp(scores - row_max)
            probabilities = (weights / jnp.sum(weights, axis=-1, keepdims=True)).astype(jnp.bfloat16)
            value_part = jnp.einsum(
                "grqk,qgrd->kgd", probabilities, d_cols, preferred_element_type=jnp.float32
            )
            return lax.dynamic_update_slice_in_dim(
                running, value_part.reshape(span_keys, k_span), group_index * k_span, 1
            )

        partial_grad = lax.fori_loop(
            0, group_count, group_step, jnp.zeros((span_keys, value_weight.shape[1]), jnp.float32)
        )

        def block_at(distance):
            return partial_grad[
                (hop_count - distance) * tok_rows : (hop_count - distance + 1) * tok_rows
            ]

        own_grad = block_at(0)
        for distance in range(1, hop_count + 1):
            sent = passed_along(block_at(distance), ALL, n_all, -distance)
            own_grad = own_grad + sent
        value_grad = own_grad.astype(jnp.bfloat16)

        spread = jnp.broadcast_to(value_grad[None], (n_fsdp,) + value_grad.shape)
        gathered = lax.all_to_all(spread, FSDP, 0, 0, tiled=True).reshape(
            n_fsdp * tok_rows, value_grad.shape[1]
        )
        local_grad = jnp.dot(inputs, gathered, preferred_element_type=jnp.float32)

        weight_full = value_weight.astype(jnp.float32)
        kept_mask = jnp.abs(weight_full) > threshold[None, :]
        signed = jnp.where(kept_mask, jnp.sign(weight_full), 0.0)

        logit_part = jnp.sum(local_grad * signed, axis=0)
        logit_sum = lax.psum(logit_part, ALL)
        grad_logit = -logit_sum * threshold * (1.0 - threshold)

        rows, cols = local_grad.shape
        piece = cols // n_seq
        pieces = local_grad.reshape(rows, n_seq, piece)
        received = lax.all_to_all(pieces, SEQ, 1, 1, tiled=True)
        dense_piece = jnp.sum(received, axis=1)
        seq_index = lax.axis_index(SEQ)
        kept_piece = lax.dynamic_slice_in_dim(kept_mask, seq_index * piece, piece, 1)
        weight_piece = jnp.where(kept_piece, dense_piece, 0.0).astype(jnp.bfloat16)
        weight_piece = lax.all_gather(weight_piece, "xh", axis=1, tiled=True)
        grad_weight = lax.all_gather(weight_piece, "z", axis=1, tiled=True)
        return (grad_weight, grad_logit)

    return local


def solution(mesh):
    names = mesh.axis_names
    assert tuple(names) == ("seq", "fsdp")
    n_seq, n_fsdp = mesh.devices.shape
    sizes = {"z": n_seq // 2, "xh": 2, "y": n_fsdp // 4, "xl": 2, "c": 2}
    phys = Mesh(
        mesh.devices.reshape([sizes[a] for a in ALL]), ALL
    )
    return jax.shard_map(
        make_local(sizes),
        mesh=phys,
        in_specs=(
            P(FSDP, SEQ),
            P(FSDP, None),
            P(),
            P(ALL, None),
            P(ALL, None),
            P(ALL, None),
        ),
        out_specs=(P(FSDP, None), P()),
        check_vma=False,
    )
```

```python
import math

import jax
import jax.numpy as jnp
from jax import lax
from jax.sharding import Mesh
from jax.sharding import PartitionSpec as P

HEAD = 128
Q_HEADS = 16
KV_HEADS = 8
WINDOW = 1024
TOK_DEV = 128


pre_scale = 168.0 ** (-0.5)
masked_score = -1e30

SEQ = ("z", "xh")
FSDP = ("y", "xl", "c")
ALL = SEQ + FSDP


def passed_along(value, axis, count, steps):
    first, last = (max(0, -steps), min(count, count - steps))
    return lax.ppermute(value, axis, [(source, source + steps) for source in range(first, last)])


def make_local(sizes):
    n_all = math.prod(sizes[a] for a in ALL)
    n_seq = math.prod(sizes[a] for a in SEQ)
    n_fsdp = math.prod(sizes[a] for a in FSDP)

    def local(inputs, value_weight, threshold, queries, keys, out_grad):
        tok_rows = queries.shape[0]
        hop_count = WINDOW // TOK_DEV
        span_keys = (hop_count + 1) * tok_rows
        head_ratio = Q_HEADS // KV_HEADS
        kv_pair = 2
        group_count = KV_HEADS // kv_pair
        position = lax.axis_index(ALL)
        earlier = [passed_along(keys, ALL, n_all, distance) for distance in range(hop_count, 0, -1)]
        key_rows = jnp.concatenate(earlier + [keys], axis=0)
        query_pos = position * tok_rows + jnp.arange(tok_rows, dtype=jnp.int32)
        key_pos = (position - hop_count) * tok_rows + jnp.arange(span_keys, dtype=jnp.int32)
        offset = query_pos[:, None] - key_pos[None, :]
        visible = (offset >= 0) & (offset < WINDOW) & (key_pos >= 0)[None, :]
        q_span = kv_pair * head_ratio * HEAD
        k_span = kv_pair * HEAD

        def group_step(group_index, running):
            q_cols = lax.dynamic_slice_in_dim(queries, group_index * q_span, q_span, 1).reshape(
                tok_rows, kv_pair, head_ratio, HEAD
            )
            d_cols = lax.dynamic_slice_in_dim(out_grad, group_index * q_span, q_span, 1).reshape(
                tok_rows, kv_pair, head_ratio, HEAD
            )
            k_cols = lax.dynamic_slice_in_dim(key_rows, group_index * k_span, k_span, 1).reshape(
                span_keys, kv_pair, HEAD
            )
            scores = (
                jnp.einsum("qgrd,kgd->grqk", q_cols, k_cols, preferred_element_type=jnp.float32)
                * pre_scale
            )
            scores = jnp.where(visible, scores, masked_score)
            row_max = jnp.max(scores, axis=-1, keepdims=True)
            weights = jnp.exp(scores - row_max)
            probabilities = (weights / jnp.sum(weights, axis=-1, keepdims=True)).astype(jnp.bfloat16)
            value_part = jnp.einsum(
                "grqk,qgrd->kgd", probabilities, d_cols, preferred_element_type=jnp.float32
            )
            return lax.dynamic_update_slice_in_dim(
                running, value_part.reshape(span_keys, k_span), group_index * k_span, 1
            )

        partial_grad = lax.fori_loop(
            0, group_count, group_step, jnp.zeros((span_keys, value_weight.shape[1]), jnp.float32)
        )

        def block_at(distance):
            return partial_grad[
                (hop_count - distance) * tok_rows : (hop_count - distance + 1) * tok_rows
            ]

        own_grad = block_at(0)
        for distance in range(1, hop_count + 1):
            sent = passed_along(block_at(distance), ALL, n_all, -distance)
            own_grad = own_grad + sent
        value_grad = own_grad.astype(jnp.bfloat16)

        spread = jnp.broadcast_to(value_grad[None], (n_fsdp,) + value_grad.shape)
        gathered = lax.all_to_all(spread, FSDP, 0, 0, tiled=True).reshape(
            n_fsdp * tok_rows, value_grad.shape[1]
        )
        local_grad = jnp.dot(inputs, gathered, preferred_element_type=jnp.float32)

        weight_full = value_weight.astype(jnp.float32)
        kept_mask = jnp.abs(weight_full) > threshold[None, :]
        signed = jnp.where(kept_mask, jnp.sign(weight_full), 0.0)

        logit_part = jnp.sum(local_grad * signed, axis=0)
        for axis in reversed(FSDP):
            logit_part = lax.psum(logit_part, axis)

        rows, cols = local_grad.shape
        piece = cols // n_seq
        payload = jnp.concatenate([local_grad, logit_part[None]], axis=0)
        pieces = payload.reshape(rows + 1, n_seq, piece)
        received = lax.all_to_all(pieces, SEQ, 1, 1, tiled=True)
        summed = jnp.sum(received, axis=1)
        dense_piece = summed[:rows]
        logit_piece = summed[rows:]
        seq_index = lax.axis_index(SEQ)
        kept_piece = lax.dynamic_slice_in_dim(kept_mask, seq_index * piece, piece, 1)
        weight_piece = jnp.where(kept_piece, dense_piece, 0.0).astype(jnp.bfloat16)
        logit_hi = logit_piece.astype(jnp.bfloat16)
        logit_lo = (logit_piece - logit_hi.astype(jnp.float32)).astype(jnp.bfloat16)
        out_piece = jnp.concatenate([weight_piece, logit_hi, logit_lo], axis=0)
        out_piece = lax.all_gather(out_piece, "xh", axis=1, tiled=True)
        out_full = lax.all_gather(out_piece, "z", axis=1, tiled=True)
        grad_weight = out_full[:rows]
        logit_sum = out_full[rows].astype(jnp.float32) + out_full[rows + 1].astype(jnp.float32)
        grad_logit = -logit_sum * threshold * (1.0 - threshold)
        return (grad_weight, grad_logit)

    return local


def solution(mesh):
    names = mesh.axis_names
    assert tuple(names) == ("seq", "fsdp")
    n_seq, n_fsdp = mesh.devices.shape
    sizes = {"z": n_seq // 2, "xh": 2, "y": n_fsdp // 4, "xl": 2, "c": 2}
    phys = Mesh(
        mesh.devices.reshape([sizes[a] for a in ALL]), ALL
    )
    return jax.shard_map(
        make_local(sizes),
        mesh=phys,
        in_specs=(
            P(FSDP, SEQ),
            P(FSDP, None),
            P(),
            P(ALL, None),
            P(ALL, None),
            P(ALL, None),
        ),
        out_specs=(P(FSDP, None), P()),
        check_vma=False,
    )
```

```python
import math

import jax
import jax.numpy as jnp
from jax import lax
from jax.sharding import Mesh
from jax.sharding import PartitionSpec as P

HEAD = 128
Q_HEADS = 16
KV_HEADS = 8
WINDOW = 1024
TOK_DEV = 128


pre_scale = 168.0 ** (-0.5)
masked_score = -1e30

SEQ = ("z", "xh")
FSDP = ("y", "xl", "c")
ALL = SEQ + FSDP


def passed_along(value, axis, count, steps):
    first, last = (max(0, -steps), min(count, count - steps))
    return lax.ppermute(value, axis, [(source, source + steps) for source in range(first, last)])


def make_local(sizes):
    n_all = math.prod(sizes[a] for a in ALL)
    n_seq = math.prod(sizes[a] for a in SEQ)
    n_fsdp = math.prod(sizes[a] for a in FSDP)

    def local(inputs, value_weight, threshold, queries, keys, out_grad):
        tok_rows = queries.shape[0]
        hop_count = WINDOW // TOK_DEV
        span_keys = (hop_count + 1) * tok_rows
        head_ratio = Q_HEADS // KV_HEADS
        kv_pair = 2
        group_count = KV_HEADS // kv_pair
        position = lax.axis_index(ALL)
        earlier = [passed_along(keys, ALL, n_all, distance) for distance in range(hop_count, 0, -1)]
        key_rows = jnp.concatenate(earlier + [keys], axis=0)
        query_pos = position * tok_rows + jnp.arange(tok_rows, dtype=jnp.int32)
        key_pos = (position - hop_count) * tok_rows + jnp.arange(span_keys, dtype=jnp.int32)
        offset = query_pos[:, None] - key_pos[None, :]
        visible = (offset >= 0) & (offset < WINDOW) & (key_pos >= 0)[None, :]
        q_span = kv_pair * head_ratio * HEAD
        k_span = kv_pair * HEAD

        def group_step(group_index, running):
            q_cols = lax.dynamic_slice_in_dim(queries, group_index * q_span, q_span, 1).reshape(
                tok_rows, kv_pair, head_ratio, HEAD
            )
            d_cols = lax.dynamic_slice_in_dim(out_grad, group_index * q_span, q_span, 1).reshape(
                tok_rows, kv_pair, head_ratio, HEAD
            )
            k_cols = lax.dynamic_slice_in_dim(key_rows, group_index * k_span, k_span, 1).reshape(
                span_keys, kv_pair, HEAD
            )
            scores = (
                jnp.einsum("qgrd,kgd->grqk", q_cols, k_cols, preferred_element_type=jnp.float32)
                * pre_scale
            )
            scores = jnp.where(visible, scores, masked_score)
            row_max = jnp.max(scores, axis=-1, keepdims=True)
            weights = jnp.exp(scores - row_max)
            probabilities = (weights / jnp.sum(weights, axis=-1, keepdims=True)).astype(jnp.bfloat16)
            value_part = jnp.einsum(
                "grqk,qgrd->kgd", probabilities, d_cols, preferred_element_type=jnp.float32
            )
            return lax.dynamic_update_slice_in_dim(
                running, value_part.reshape(span_keys, k_span), group_index * k_span, 1
            )

        partial_grad = lax.fori_loop(
            0, group_count, group_step, jnp.zeros((span_keys, value_weight.shape[1]), jnp.float32)
        )

        def block_at(distance):
            return partial_grad[
                (hop_count - distance) * tok_rows : (hop_count - distance + 1) * tok_rows
            ]

        own_grad = block_at(0)
        for distance in range(1, hop_count + 1):
            sent = passed_along(block_at(distance).astype(jnp.bfloat16), ALL, n_all, -distance)
            own_grad = own_grad + sent.astype(jnp.float32)
        value_grad = own_grad.astype(jnp.bfloat16)

        spread = jnp.broadcast_to(value_grad[None], (n_fsdp,) + value_grad.shape)
        gathered = lax.all_to_all(spread, FSDP, 0, 0, tiled=True).reshape(
            n_fsdp * tok_rows, value_grad.shape[1]
        )
        local_grad = jnp.dot(inputs, gathered, preferred_element_type=jnp.float32)

        weight_full = value_weight.astype(jnp.float32)
        kept_mask = jnp.abs(weight_full) > threshold[None, :]
        signed = jnp.where(kept_mask, jnp.sign(weight_full), 0.0)

        logit_part = jnp.sum(local_grad * signed, axis=0)
        for axis in reversed(FSDP):
            logit_part = lax.psum(logit_part, axis)

        rows, cols = local_grad.shape
        piece = cols // n_seq
        payload = jnp.concatenate([local_grad, logit_part[None]], axis=0)
        pieces = payload.reshape(rows + 1, n_seq, piece)
        received = lax.all_to_all(pieces, SEQ, 1, 1, tiled=True)
        summed = jnp.sum(received, axis=1)
        dense_piece = summed[:rows]
        logit_piece = summed[rows:]
        seq_index = lax.axis_index(SEQ)
        kept_piece = lax.dynamic_slice_in_dim(kept_mask, seq_index * piece, piece, 1)
        weight_piece = jnp.where(kept_piece, dense_piece, 0.0).astype(jnp.bfloat16)
        logit_hi = logit_piece.astype(jnp.bfloat16)
        logit_lo = (logit_piece - logit_hi.astype(jnp.float32)).astype(jnp.bfloat16)
        out_piece = jnp.concatenate([weight_piece, logit_hi, logit_lo], axis=0)
        out_piece = lax.all_gather(out_piece, "xh", axis=1, tiled=True)
        out_full = lax.all_gather(out_piece, "z", axis=1, tiled=True)
        grad_weight = out_full[:rows]
        logit_sum = out_full[rows].astype(jnp.float32) + out_full[rows + 1].astype(jnp.float32)
        grad_logit = -logit_sum * threshold * (1.0 - threshold)
        return (grad_weight, grad_logit)

    return local


def solution(mesh):
    names = mesh.axis_names
    assert tuple(names) == ("seq", "fsdp")
    n_seq, n_fsdp = mesh.devices.shape
    sizes = {"z": n_seq // 2, "xh": 2, "y": n_fsdp // 4, "xl": 2, "c": 2}
    phys = Mesh(
        mesh.devices.reshape([sizes[a] for a in ALL]), ALL
    )
    return jax.shard_map(
        make_local(sizes),
        mesh=phys,
        in_specs=(
            P(FSDP, SEQ),
            P(FSDP, None),
            P(),
            P(ALL, None),
            P(ALL, None),
            P(ALL, None),
        ),
        out_specs=(P(FSDP, None), P()),
        check_vma=False,
    )
```

```python
import math

import jax
import jax.numpy as jnp
from jax import lax
from jax.sharding import Mesh
from jax.sharding import PartitionSpec as P

HEAD = 128
Q_HEADS = 16
KV_HEADS = 8
WINDOW = 1024
TOK_DEV = 128


pre_scale = 168.0 ** (-0.5)
masked_score = -1e30

SEQ = ("z", "xh")
FSDP = ("y", "xl", "c")
ALL = SEQ + FSDP


def passed_along(value, axis, count, steps):
    first, last = (max(0, -steps), min(count, count - steps))
    return lax.ppermute(value, axis, [(source, source + steps) for source in range(first, last)])


def make_local(sizes):
    n_all = math.prod(sizes[a] for a in ALL)
    n_seq = math.prod(sizes[a] for a in SEQ)
    n_fsdp = math.prod(sizes[a] for a in FSDP)

    def local(inputs, value_weight, threshold, queries, keys, out_grad):
        tok_rows = queries.shape[0]
        hop_count = WINDOW // TOK_DEV
        span_keys = (hop_count + 1) * tok_rows
        head_ratio = Q_HEADS // KV_HEADS
        kv_pair = 2
        group_count = KV_HEADS // kv_pair
        position = lax.axis_index(ALL)
        earlier = [passed_along(keys, ALL, n_all, distance) for distance in range(hop_count, 0, -1)]
        key_rows = jnp.concatenate(earlier + [keys], axis=0)
        query_pos = position * tok_rows + jnp.arange(tok_rows, dtype=jnp.int32)
        key_pos = (position - hop_count) * tok_rows + jnp.arange(span_keys, dtype=jnp.int32)
        offset = query_pos[:, None] - key_pos[None, :]
        visible = (offset >= 0) & (offset < WINDOW) & (key_pos >= 0)[None, :]
        q_span = kv_pair * head_ratio * HEAD
        k_span = kv_pair * HEAD

        def group_step(group_index, running):
            q_cols = lax.dynamic_slice_in_dim(queries, group_index * q_span, q_span, 1).reshape(
                tok_rows, kv_pair, head_ratio, HEAD
            )
            d_cols = lax.dynamic_slice_in_dim(out_grad, group_index * q_span, q_span, 1).reshape(
                tok_rows, kv_pair, head_ratio, HEAD
            )
            k_cols = lax.dynamic_slice_in_dim(key_rows, group_index * k_span, k_span, 1).reshape(
                span_keys, kv_pair, HEAD
            )
            scores = (
                jnp.einsum("qgrd,kgd->grqk", q_cols, k_cols, preferred_element_type=jnp.float32)
                * pre_scale
            )
            scores = jnp.where(visible, scores, masked_score)
            row_max = jnp.max(scores, axis=-1, keepdims=True)
            weights = jnp.exp(scores - row_max)
            probabilities = (weights / jnp.sum(weights, axis=-1, keepdims=True)).astype(jnp.bfloat16)
            value_part = jnp.einsum(
                "grqk,qgrd->kgd", probabilities, d_cols, preferred_element_type=jnp.float32
            )
            return lax.dynamic_update_slice_in_dim(
                running, value_part.reshape(span_keys, k_span), group_index * k_span, 1
            )

        weight_full = value_weight.astype(jnp.float32)
        kept_mask = jnp.abs(weight_full) > threshold[None, :]
        signed = jnp.where(kept_mask, jnp.sign(weight_full), 0.0)
        seq_index = lax.axis_index(SEQ)
        n_chunks = 2
        chunk_groups = group_count // n_chunks
        chunk_cols = chunk_groups * k_span
        rows = inputs.shape[0]

        local_parts = []
        for chunk in range(n_chunks):
            def chunk_step(step, running, chunk=chunk):
                return group_step(chunk * chunk_groups + step, running)

            partial_grad = lax.fori_loop(
                0,
                chunk_groups,
                chunk_step,
                jnp.zeros((span_keys, value_weight.shape[1]), jnp.float32),
            )
            partial_grad = partial_grad[:, chunk * chunk_cols : (chunk + 1) * chunk_cols]

            def block_at(distance):
                return partial_grad[
                    (hop_count - distance) * tok_rows : (hop_count - distance + 1) * tok_rows
                ]

            own_grad = block_at(0)
            for distance in range(1, hop_count + 1):
                sent = passed_along(block_at(distance).astype(jnp.bfloat16), ALL, n_all, -distance)
                own_grad = own_grad + sent.astype(jnp.float32)
            value_grad = own_grad.astype(jnp.bfloat16)

            spread = jnp.broadcast_to(value_grad[None], (n_fsdp,) + value_grad.shape)
            gathered = lax.all_to_all(spread, FSDP, 0, 0, tiled=True).reshape(
                n_fsdp * tok_rows, chunk_cols
            )
            local_grad = jnp.dot(inputs, gathered, preferred_element_type=jnp.float32)
            local_parts.append(local_grad)

        local_grad = jnp.concatenate(local_parts, axis=1)
        piece = local_grad.shape[1] // n_seq

        logit_part = jnp.sum(local_grad * signed, axis=0)
        for axis in reversed(FSDP):
            logit_part = lax.psum(logit_part, axis)

        payload = jnp.concatenate([local_grad, logit_part[None]], axis=0)
        pieces = payload.reshape(rows + 1, n_seq, piece)
        received = lax.all_to_all(pieces, SEQ, 1, 1, tiled=True)
        summed = jnp.sum(received, axis=1)
        dense_piece = summed[:rows]
        logit_piece = summed[rows:]
        kept_piece = lax.dynamic_slice_in_dim(kept_mask, seq_index * piece, piece, 1)
        weight_piece = jnp.where(kept_piece, dense_piece, 0.0).astype(jnp.bfloat16)
        logit_hi = logit_piece.astype(jnp.bfloat16)
        logit_lo = (logit_piece - logit_hi.astype(jnp.float32)).astype(jnp.bfloat16)
        out_piece = jnp.concatenate([weight_piece, logit_hi, logit_lo], axis=0)
        out_piece = lax.all_gather(out_piece, "xh", axis=1, tiled=True)
        out_full = lax.all_gather(out_piece, "z", axis=1, tiled=True)
        grad_weight = out_full[:rows]
        logit_sum = out_full[rows].astype(jnp.float32) + out_full[rows + 1].astype(jnp.float32)
        grad_logit = -logit_sum * threshold * (1.0 - threshold)
        return (grad_weight, grad_logit)

    return local


def solution(mesh):
    names = mesh.axis_names
    assert tuple(names) == ("seq", "fsdp")
    n_seq, n_fsdp = mesh.devices.shape
    sizes = {"z": n_seq // 2, "xh": 2, "y": n_fsdp // 4, "xl": 2, "c": 2}
    phys = Mesh(
        mesh.devices.reshape([sizes[a] for a in ALL]), ALL
    )
    return jax.shard_map(
        make_local(sizes),
        mesh=phys,
        in_specs=(
            P(FSDP, SEQ),
            P(FSDP, None),
            P(),
            P(ALL, None),
            P(ALL, None),
            P(ALL, None),
        ),
        out_specs=(P(FSDP, None), P()),
        check_vma=False,
    )
```

```python
import math

import jax
import jax.numpy as jnp
from jax import lax
from jax.sharding import Mesh
from jax.sharding import PartitionSpec as P

HEAD = 128
Q_HEADS = 16
KV_HEADS = 8
WINDOW = 1024
TOK_DEV = 128


pre_scale = 168.0 ** (-0.5)
masked_score = -1e30

SEQ = ("z", "xh")
FSDP = ("y", "xl", "c")
ALL = SEQ + FSDP


def passed_along(value, axis, count, steps):
    first, last = (max(0, -steps), min(count, count - steps))
    return lax.ppermute(value, axis, [(source, source + steps) for source in range(first, last)])


def make_local(sizes):
    n_all = math.prod(sizes[a] for a in ALL)
    n_seq = math.prod(sizes[a] for a in SEQ)
    n_fsdp = math.prod(sizes[a] for a in FSDP)

    def local(inputs, value_weight, threshold, queries, keys, out_grad):
        tok_rows = queries.shape[0]
        hop_count = WINDOW // TOK_DEV
        span_keys = (hop_count + 1) * tok_rows
        head_ratio = Q_HEADS // KV_HEADS
        kv_pair = 2
        group_count = KV_HEADS // kv_pair
        position = lax.axis_index(ALL)
        earlier = [passed_along(keys, ALL, n_all, distance) for distance in range(hop_count, 0, -1)]
        key_rows = jnp.concatenate(earlier + [keys], axis=0)
        query_pos = position * tok_rows + jnp.arange(tok_rows, dtype=jnp.int32)
        key_pos = (position - hop_count) * tok_rows + jnp.arange(span_keys, dtype=jnp.int32)
        offset = query_pos[:, None] - key_pos[None, :]
        visible = (offset >= 0) & (offset < WINDOW) & (key_pos >= 0)[None, :]
        q_span = kv_pair * head_ratio * HEAD
        k_span = kv_pair * HEAD

        def group_step(group_index, running):
            q_cols = lax.dynamic_slice_in_dim(queries, group_index * q_span, q_span, 1).reshape(
                tok_rows, kv_pair, head_ratio, HEAD
            )
            d_cols = lax.dynamic_slice_in_dim(out_grad, group_index * q_span, q_span, 1).reshape(
                tok_rows, kv_pair, head_ratio, HEAD
            )
            k_cols = lax.dynamic_slice_in_dim(key_rows, group_index * k_span, k_span, 1).reshape(
                span_keys, kv_pair, HEAD
            )
            scores = (
                jnp.einsum("qgrd,kgd->grqk", q_cols, k_cols, preferred_element_type=jnp.float32)
                * pre_scale
            )
            scores = jnp.where(visible, scores, masked_score)
            row_max = jnp.max(scores, axis=-1, keepdims=True)
            weights = jnp.exp(scores - row_max)
            probabilities = (weights / jnp.sum(weights, axis=-1, keepdims=True)).astype(jnp.bfloat16)
            value_part = jnp.einsum(
                "grqk,qgrd->kgd", probabilities, d_cols, preferred_element_type=jnp.float32
            )
            return lax.dynamic_update_slice_in_dim(
                running, value_part.reshape(span_keys, k_span), group_index * k_span, 1
            )

        partial_grad = lax.fori_loop(
            0, group_count, group_step, jnp.zeros((span_keys, value_weight.shape[1]), jnp.float32)
        )

        def block_at(distance):
            return partial_grad[
                (hop_count - distance) * tok_rows : (hop_count - distance + 1) * tok_rows
            ]

        own_grad = block_at(0)
        for distance in range(1, hop_count + 1):
            sent = passed_along(block_at(distance).astype(jnp.bfloat16), ALL, n_all, -distance)
            own_grad = own_grad + sent.astype(jnp.float32)
        value_grad = own_grad.astype(jnp.bfloat16)

        spread = jnp.broadcast_to(value_grad[None], (n_fsdp,) + value_grad.shape)
        gathered = lax.all_to_all(spread, FSDP, 0, 0, tiled=True).reshape(
            n_fsdp * tok_rows, value_grad.shape[1]
        )
        local_grad = jnp.dot(inputs, gathered, preferred_element_type=jnp.float32)

        weight_full = value_weight.astype(jnp.float32)
        kept_mask = jnp.abs(weight_full) > threshold[None, :]
        signed = jnp.where(kept_mask, jnp.sign(weight_full), 0.0)

        logit_part = jnp.sum(local_grad * signed, axis=0)

        rows, cols = local_grad.shape
        piece = cols // n_seq
        pieces = local_grad.reshape(rows, n_seq, piece)
        received = lax.all_to_all(pieces, SEQ, 1, 1, tiled=True)
        for axis in reversed(ALL):
            logit_part = lax.psum(logit_part, axis)
        grad_logit = -logit_part * threshold * (1.0 - threshold)

        dense_piece = jnp.sum(received, axis=1)
        seq_index = lax.axis_index(SEQ)
        kept_piece = lax.dynamic_slice_in_dim(kept_mask, seq_index * piece, piece, 1)
        weight_piece = jnp.where(kept_piece, dense_piece, 0.0).astype(jnp.bfloat16)
        weight_piece = lax.all_gather(weight_piece, "xh", axis=1, tiled=True)
        grad_weight = lax.all_gather(weight_piece, "z", axis=1, tiled=True)
        return (grad_weight, grad_logit)

    return local


def solution(mesh):
    names = mesh.axis_names
    assert tuple(names) == ("seq", "fsdp")
    n_seq, n_fsdp = mesh.devices.shape
    sizes = {"z": n_seq // 2, "xh": 2, "y": n_fsdp // 4, "xl": 2, "c": 2}
    phys = Mesh(
        mesh.devices.reshape([sizes[a] for a in ALL]), ALL
    )
    return jax.shard_map(
        make_local(sizes),
        mesh=phys,
        in_specs=(
            P(FSDP, SEQ),
            P(FSDP, None),
            P(),
            P(ALL, None),
            P(ALL, None),
            P(ALL, None),
        ),
        out_specs=(P(FSDP, None), P()),
        check_vma=False,
    )
```

```python
import math

import jax
import jax.numpy as jnp
from jax import lax
from jax.sharding import Mesh
from jax.sharding import PartitionSpec as P

HEAD = 128
Q_HEADS = 16
KV_HEADS = 8
WINDOW = 1024
TOK_DEV = 128


pre_scale = 168.0 ** (-0.5)
masked_score = -1e30

SEQ = ("z", "xh")
FSDP = ("y", "xl", "c")
ALL = SEQ + FSDP


def passed_along(value, axis, count, steps):
    first, last = (max(0, -steps), min(count, count - steps))
    return lax.ppermute(value, axis, [(source, source + steps) for source in range(first, last)])


def make_local(sizes):
    n_all = math.prod(sizes[a] for a in ALL)
    n_seq = math.prod(sizes[a] for a in SEQ)
    n_fsdp = math.prod(sizes[a] for a in FSDP)

    def local(inputs, value_weight, threshold, queries, keys, out_grad):
        tok_rows = queries.shape[0]
        hop_count = WINDOW // TOK_DEV
        span_keys = (hop_count + 1) * tok_rows
        head_ratio = Q_HEADS // KV_HEADS
        kv_pair = 2
        group_count = KV_HEADS // kv_pair
        position = lax.axis_index(ALL)
        earlier = [passed_along(keys, ALL, n_all, distance) for distance in range(hop_count, 0, -1)]
        key_rows = jnp.concatenate(earlier + [keys], axis=0)
        query_pos = position * tok_rows + jnp.arange(tok_rows, dtype=jnp.int32)
        key_pos = (position - hop_count) * tok_rows + jnp.arange(span_keys, dtype=jnp.int32)
        offset = query_pos[:, None] - key_pos[None, :]
        visible = (offset >= 0) & (offset < WINDOW) & (key_pos >= 0)[None, :]
        q_span = kv_pair * head_ratio * HEAD
        k_span = kv_pair * HEAD

        def group_step(group_index, running):
            q_cols = lax.dynamic_slice_in_dim(queries, group_index * q_span, q_span, 1).reshape(
                tok_rows, kv_pair, head_ratio, HEAD
            )
            d_cols = lax.dynamic_slice_in_dim(out_grad, group_index * q_span, q_span, 1).reshape(
                tok_rows, kv_pair, head_ratio, HEAD
            )
            k_cols = lax.dynamic_slice_in_dim(key_rows, group_index * k_span, k_span, 1).reshape(
                span_keys, kv_pair, HEAD
            )
            scores = (
                jnp.einsum("qgrd,kgd->grqk", q_cols, k_cols, preferred_element_type=jnp.float32)
                * pre_scale
            )
            scores = jnp.where(visible, scores, masked_score)
            row_max = jnp.max(scores, axis=-1, keepdims=True)
            weights = jnp.exp(scores - row_max)
            probabilities = (weights / jnp.sum(weights, axis=-1, keepdims=True)).astype(jnp.bfloat16)
            value_part = jnp.einsum(
                "grqk,qgrd->kgd", probabilities, d_cols, preferred_element_type=jnp.float32
            )
            return lax.dynamic_update_slice_in_dim(
                running, value_part.reshape(span_keys, k_span), group_index * k_span, 1
            )

        partial_grad = lax.fori_loop(
            0, group_count, group_step, jnp.zeros((span_keys, value_weight.shape[1]), jnp.float32)
        )

        def block_at(distance):
            return partial_grad[
                (hop_count - distance) * tok_rows : (hop_count - distance + 1) * tok_rows
            ]

        own_grad = block_at(0)
        for distance in range(1, hop_count + 1):
            sent = passed_along(block_at(distance).astype(jnp.bfloat16), ALL, n_all, -distance)
            own_grad = own_grad + sent.astype(jnp.float32)
        value_grad = own_grad.astype(jnp.bfloat16)

        spread = jnp.broadcast_to(value_grad[None], (n_fsdp,) + value_grad.shape)
        gathered = lax.all_to_all(spread, FSDP, 0, 0, tiled=True).reshape(
            n_fsdp * tok_rows, value_grad.shape[1]
        )
        local_grad = jnp.dot(inputs, gathered, preferred_element_type=jnp.float32)

        weight_full = value_weight.astype(jnp.float32)
        kept_mask = jnp.abs(weight_full) > threshold[None, :]
        signed = jnp.where(kept_mask, jnp.sign(weight_full), 0.0)

        logit_part = jnp.sum(local_grad * signed, axis=0)

        rows, cols = local_grad.shape
        n_z = lax.axis_size("z")
        half = cols // 2
        piece = half // n_z
        xh_index = lax.axis_index("xh")
        keep = lax.dynamic_slice_in_dim(local_grad, xh_index * half, half, 1)
        send = lax.dynamic_slice_in_dim(local_grad, (1 - xh_index) * half, half, 1)
        swapped = keep + lax.ppermute(send, "xh", [(0, 1), (1, 0)])
        for axis in ("c", "xl", "y", "xh"):
            logit_part = lax.psum(logit_part, axis)
        logit_half = lax.dynamic_slice_in_dim(logit_part, xh_index * half, half, 0)
        payload = jnp.concatenate([swapped, logit_half[None]], axis=0)
        received = lax.all_to_all(payload.reshape(rows + 1, n_z, piece), "z", 1, 1, tiled=True)
        summed = jnp.sum(received, axis=1)
        dense_piece = summed[:rows]
        logit_piece = summed[rows:]
        z_index = lax.axis_index("z")
        kept_piece = lax.dynamic_slice_in_dim(
            kept_mask, xh_index * half + z_index * piece, piece, 1
        )
        weight_piece = jnp.where(kept_piece, dense_piece, 0.0).astype(jnp.bfloat16)
        logit_hi = logit_piece.astype(jnp.bfloat16)
        logit_lo = (logit_piece - logit_hi.astype(jnp.float32)).astype(jnp.bfloat16)
        out_piece = jnp.concatenate([weight_piece, logit_hi, logit_lo], axis=0)
        out_piece = lax.all_gather(out_piece, "z", axis=1, tiled=True)
        out_full = lax.all_gather(out_piece, "xh", axis=1, tiled=True)
        grad_weight = out_full[:rows]
        logit_sum = out_full[rows].astype(jnp.float32) + out_full[rows + 1].astype(jnp.float32)
        grad_logit = -logit_sum * threshold * (1.0 - threshold)
        return (grad_weight, grad_logit)

    return local


def solution(mesh):
    names = mesh.axis_names
    assert tuple(names) == ("seq", "fsdp")
    n_seq, n_fsdp = mesh.devices.shape
    sizes = {"z": n_seq // 2, "xh": 2, "y": n_fsdp // 4, "xl": 2, "c": 2}
    phys = Mesh(
        mesh.devices.reshape([sizes[a] for a in ALL]), ALL
    )
    return jax.shard_map(
        make_local(sizes),
        mesh=phys,
        in_specs=(
            P(FSDP, SEQ),
            P(FSDP, None),
            P(),
            P(ALL, None),
            P(ALL, None),
            P(ALL, None),
        ),
        out_specs=(P(FSDP, None), P()),
        check_vma=False,
    )
```

```python
import math

import jax
import jax.numpy as jnp
from jax import lax
from jax.sharding import Mesh
from jax.sharding import PartitionSpec as P

HEAD = 128
Q_HEADS = 16
KV_HEADS = 8
WINDOW = 1024
TOK_DEV = 128


pre_scale = 168.0 ** (-0.5)
masked_score = -1e30

SEQ = ("z", "xh")
FSDP = ("y", "xl", "c")
ALL = SEQ + FSDP


def passed_along(value, axis, count, steps):
    first, last = (max(0, -steps), min(count, count - steps))
    return lax.ppermute(value, axis, [(source, source + steps) for source in range(first, last)])


def make_local(sizes):
    n_all = math.prod(sizes[a] for a in ALL)
    n_seq = math.prod(sizes[a] for a in SEQ)
    n_fsdp = math.prod(sizes[a] for a in FSDP)

    def local(inputs, value_weight, threshold, queries, keys, out_grad):
        tok_rows = queries.shape[0]
        hop_count = WINDOW // TOK_DEV
        span_keys = (hop_count + 1) * tok_rows
        head_ratio = Q_HEADS // KV_HEADS
        kv_pair = 2
        group_count = KV_HEADS // kv_pair
        position = lax.axis_index(ALL)
        earlier = [passed_along(keys, ALL, n_all, distance) for distance in range(hop_count, 0, -1)]
        key_rows = jnp.concatenate(earlier + [keys], axis=0)
        query_pos = position * tok_rows + jnp.arange(tok_rows, dtype=jnp.int32)
        key_pos = (position - hop_count) * tok_rows + jnp.arange(span_keys, dtype=jnp.int32)
        offset = query_pos[:, None] - key_pos[None, :]
        visible = (offset >= 0) & (offset < WINDOW) & (key_pos >= 0)[None, :]
        q_span = kv_pair * head_ratio * HEAD
        k_span = kv_pair * HEAD

        value_parts = []
        for group_index in range(group_count):
            q_cols = queries[:, group_index * q_span : (group_index + 1) * q_span].reshape(
                tok_rows, kv_pair, head_ratio, HEAD
            )
            d_cols = out_grad[:, group_index * q_span : (group_index + 1) * q_span].reshape(
                tok_rows, kv_pair, head_ratio, HEAD
            )
            k_cols = key_rows[:, group_index * k_span : (group_index + 1) * k_span].reshape(
                span_keys, kv_pair, HEAD
            )
            scores = (
                jnp.einsum("qgrd,kgd->grqk", q_cols, k_cols, preferred_element_type=jnp.float32)
                * pre_scale
            )
            scores = jnp.where(visible, scores, masked_score)
            row_max = jnp.max(scores, axis=-1, keepdims=True)
            weights = jnp.exp(scores - row_max)
            probabilities = (weights / jnp.sum(weights, axis=-1, keepdims=True)).astype(jnp.bfloat16)
            value_part = jnp.einsum(
                "grqk,qgrd->kgd", probabilities, d_cols, preferred_element_type=jnp.float32
            )
            value_parts.append(value_part.reshape(span_keys, k_span))

        partial_grad = jnp.concatenate(value_parts, axis=1)

        def block_at(distance):
            return partial_grad[
                (hop_count - distance) * tok_rows : (hop_count - distance + 1) * tok_rows
            ]

        own_grad = block_at(0)
        for distance in range(1, hop_count + 1):
            sent = passed_along(block_at(distance).astype(jnp.bfloat16), ALL, n_all, -distance)
            own_grad = own_grad + sent.astype(jnp.float32)
        value_grad = own_grad.astype(jnp.bfloat16)

        spread = jnp.broadcast_to(value_grad[None], (n_fsdp,) + value_grad.shape)
        gathered = lax.all_to_all(spread, FSDP, 0, 0, tiled=True).reshape(
            n_fsdp * tok_rows, value_grad.shape[1]
        )
        local_grad = jnp.dot(inputs, gathered, preferred_element_type=jnp.float32)

        weight_full = value_weight.astype(jnp.float32)
        kept_mask = jnp.abs(weight_full) > threshold[None, :]
        signed = jnp.where(kept_mask, jnp.sign(weight_full), 0.0)

        logit_part = jnp.sum(local_grad * signed, axis=0)

        rows, cols = local_grad.shape
        n_z = lax.axis_size("z")
        half = cols // 2
        piece = half // n_z
        xh_index = lax.axis_index("xh")
        keep = lax.dynamic_slice_in_dim(local_grad, xh_index * half, half, 1)
        send = lax.dynamic_slice_in_dim(local_grad, (1 - xh_index) * half, half, 1)
        swapped = keep + lax.ppermute(send, "xh", [(0, 1), (1, 0)])
        for axis in ("c", "xl", "y", "xh"):
            logit_part = lax.psum(logit_part, axis)
        logit_half = lax.dynamic_slice_in_dim(logit_part, xh_index * half, half, 0)
        payload = jnp.concatenate([swapped, logit_half[None]], axis=0)
        received = lax.all_to_all(payload.reshape(rows + 1, n_z, piece), "z", 1, 1, tiled=True)
        summed = jnp.sum(received, axis=1)
        dense_piece = summed[:rows]
        logit_piece = summed[rows:]
        z_index = lax.axis_index("z")
        kept_piece = lax.dynamic_slice_in_dim(
            kept_mask, xh_index * half + z_index * piece, piece, 1
        )
        weight_piece = jnp.where(kept_piece, dense_piece, 0.0).astype(jnp.bfloat16)
        logit_hi = logit_piece.astype(jnp.bfloat16)
        logit_lo = (logit_piece - logit_hi.astype(jnp.float32)).astype(jnp.bfloat16)
        out_piece = jnp.concatenate([weight_piece, logit_hi, logit_lo], axis=0)
        out_piece = lax.all_gather(out_piece, "z", axis=1, tiled=True)
        out_full = lax.all_gather(out_piece, "xh", axis=1, tiled=True)
        grad_weight = out_full[:rows]
        logit_sum = out_full[rows].astype(jnp.float32) + out_full[rows + 1].astype(jnp.float32)
        grad_logit = -logit_sum * threshold * (1.0 - threshold)
        return (grad_weight, grad_logit)

    return local


def solution(mesh):
    names = mesh.axis_names
    assert tuple(names) == ("seq", "fsdp")
    n_seq, n_fsdp = mesh.devices.shape
    sizes = {"z": n_seq // 2, "xh": 2, "y": n_fsdp // 4, "xl": 2, "c": 2}
    phys = Mesh(
        mesh.devices.reshape([sizes[a] for a in ALL]), ALL
    )
    return jax.shard_map(
        make_local(sizes),
        mesh=phys,
        in_specs=(
            P(FSDP, SEQ),
            P(FSDP, None),
            P(),
            P(ALL, None),
            P(ALL, None),
            P(ALL, None),
        ),
        out_specs=(P(FSDP, None), P()),
        check_vma=False,
    )
```

```python
import math

import jax
import jax.numpy as jnp
from jax import lax
from jax.sharding import Mesh
from jax.sharding import PartitionSpec as P

HEAD = 128
Q_HEADS = 16
KV_HEADS = 8
WINDOW = 1024
TOK_DEV = 128


pre_scale = 168.0 ** (-0.5)
masked_score = -1e30

SEQ = ("z", "xh")
FSDP = ("y", "xl", "c")
ALL = SEQ + FSDP


def passed_along(value, axis, count, steps):
    first, last = (max(0, -steps), min(count, count - steps))
    return lax.ppermute(value, axis, [(source, source + steps) for source in range(first, last)])


def doubling_gather(value, axis, count, index):
    step = 1
    while step < count:
        other = lax.ppermute(value, axis, [(i, i ^ step) for i in range(count)])
        low = (index & step) == 0
        value = jnp.where(
            low, jnp.concatenate([value, other], axis=1), jnp.concatenate([other, value], axis=1)
        )
        step *= 2
    return value


def make_local(sizes):
    n_all = math.prod(sizes[a] for a in ALL)
    n_seq = math.prod(sizes[a] for a in SEQ)
    n_fsdp = math.prod(sizes[a] for a in FSDP)

    def local(inputs, value_weight, threshold, queries, keys, out_grad):
        tok_rows = queries.shape[0]
        hop_count = WINDOW // TOK_DEV
        span_keys = (hop_count + 1) * tok_rows
        head_ratio = Q_HEADS // KV_HEADS
        kv_pair = 2
        group_count = KV_HEADS // kv_pair
        position = lax.axis_index(ALL)
        earlier = [passed_along(keys, ALL, n_all, distance) for distance in range(hop_count, 0, -1)]
        key_rows = jnp.concatenate(earlier + [keys], axis=0)
        query_pos = position * tok_rows + jnp.arange(tok_rows, dtype=jnp.int32)
        key_pos = (position - hop_count) * tok_rows + jnp.arange(span_keys, dtype=jnp.int32)
        offset = query_pos[:, None] - key_pos[None, :]
        visible = (offset >= 0) & (offset < WINDOW) & (key_pos >= 0)[None, :]
        q_span = kv_pair * head_ratio * HEAD
        k_span = kv_pair * HEAD

        value_parts = []
        for group_index in range(group_count):
            q_cols = queries[:, group_index * q_span : (group_index + 1) * q_span].reshape(
                tok_rows, kv_pair, head_ratio, HEAD
            )
            d_cols = out_grad[:, group_index * q_span : (group_index + 1) * q_span].reshape(
                tok_rows, kv_pair, head_ratio, HEAD
            )
            k_cols = key_rows[:, group_index * k_span : (group_index + 1) * k_span].reshape(
                span_keys, kv_pair, HEAD
            )
            scores = (
                jnp.einsum("qgrd,kgd->grqk", q_cols, k_cols, preferred_element_type=jnp.float32)
                * pre_scale
            )
            scores = jnp.where(visible, scores, masked_score)
            row_max = jnp.max(scores, axis=-1, keepdims=True)
            weights = jnp.exp(scores - row_max)
            probabilities = (weights / jnp.sum(weights, axis=-1, keepdims=True)).astype(jnp.bfloat16)
            value_part = jnp.einsum(
                "grqk,qgrd->kgd", probabilities, d_cols, preferred_element_type=jnp.float32
            )
            value_parts.append(value_part.reshape(span_keys, k_span))

        partial_grad = jnp.concatenate(value_parts, axis=1)

        def block_at(distance):
            return partial_grad[
                (hop_count - distance) * tok_rows : (hop_count - distance + 1) * tok_rows
            ]

        own_grad = block_at(0)
        for distance in range(1, hop_count + 1):
            sent = passed_along(block_at(distance).astype(jnp.bfloat16), ALL, n_all, -distance)
            own_grad = own_grad + sent.astype(jnp.float32)
        value_grad = own_grad.astype(jnp.bfloat16)

        spread = jnp.broadcast_to(value_grad[None], (n_fsdp,) + value_grad.shape)
        gathered = lax.all_to_all(spread, FSDP, 0, 0, tiled=True).reshape(
            n_fsdp * tok_rows, value_grad.shape[1]
        )
        local_grad = jnp.dot(inputs, gathered, preferred_element_type=jnp.float32)

        weight_full = value_weight.astype(jnp.float32)
        kept_mask = jnp.abs(weight_full) > threshold[None, :]
        signed = jnp.where(kept_mask, jnp.sign(weight_full), 0.0)

        logit_part = jnp.sum(local_grad * signed, axis=0)

        rows, cols = local_grad.shape
        n_z = lax.axis_size("z")
        half = cols // 2
        piece = half // n_z
        xh_index = lax.axis_index("xh")
        keep = lax.dynamic_slice_in_dim(local_grad, xh_index * half, half, 1)
        send = lax.dynamic_slice_in_dim(local_grad, (1 - xh_index) * half, half, 1)
        swapped = keep + lax.ppermute(send, "xh", [(0, 1), (1, 0)])
        for axis in ("c", "xl", "y", "xh"):
            logit_part = lax.psum(logit_part, axis)
        logit_half = lax.dynamic_slice_in_dim(logit_part, xh_index * half, half, 0)
        payload = jnp.concatenate([swapped, logit_half[None]], axis=0)
        received = lax.all_to_all(payload.reshape(rows + 1, n_z, piece), "z", 1, 1, tiled=True)
        summed = jnp.sum(received, axis=1)
        dense_piece = summed[:rows]
        logit_piece = summed[rows:]
        z_index = lax.axis_index("z")
        kept_piece = lax.dynamic_slice_in_dim(
            kept_mask, xh_index * half + z_index * piece, piece, 1
        )
        weight_piece = jnp.where(kept_piece, dense_piece, 0.0).astype(jnp.bfloat16)
        logit_hi = logit_piece.astype(jnp.bfloat16)
        logit_lo = (logit_piece - logit_hi.astype(jnp.float32)).astype(jnp.bfloat16)
        out_piece = jnp.concatenate([weight_piece, logit_hi, logit_lo], axis=0)
        out_full = doubling_gather(out_piece, "z", n_z, z_index)
        out_full = doubling_gather(out_full, "xh", 2, xh_index)
        grad_weight = out_full[:rows]
        logit_sum = out_full[rows].astype(jnp.float32) + out_full[rows + 1].astype(jnp.float32)
        grad_logit = -logit_sum * threshold * (1.0 - threshold)
        return (grad_weight, grad_logit)

    return local


def solution(mesh):
    names = mesh.axis_names
    assert tuple(names) == ("seq", "fsdp")
    n_seq, n_fsdp = mesh.devices.shape
    sizes = {"z": n_seq // 2, "xh": 2, "y": n_fsdp // 4, "xl": 2, "c": 2}
    phys = Mesh(
        mesh.devices.reshape([sizes[a] for a in ALL]), ALL
    )
    return jax.shard_map(
        make_local(sizes),
        mesh=phys,
        in_specs=(
            P(FSDP, SEQ),
            P(FSDP, None),
            P(),
            P(ALL, None),
            P(ALL, None),
            P(ALL, None),
        ),
        out_specs=(P(FSDP, None), P()),
        check_vma=False,
    )
```

```python
import math

import jax
import jax.numpy as jnp
from jax import lax
from jax.sharding import Mesh
from jax.sharding import PartitionSpec as P

HEAD = 128
Q_HEADS = 16
KV_HEADS = 8
WINDOW = 1024
TOK_DEV = 128


pre_scale = 168.0 ** (-0.5)
masked_score = -1e30

SEQ = ("z", "xh")
FSDP = ("y", "xl", "c")
ALL = SEQ + FSDP


def passed_along(value, axis, count, steps):
    first, last = (max(0, -steps), min(count, count - steps))
    return lax.ppermute(value, axis, [(source, source + steps) for source in range(first, last)])


def make_local(sizes):
    n_all = math.prod(sizes[a] for a in ALL)
    n_seq = math.prod(sizes[a] for a in SEQ)
    n_fsdp = math.prod(sizes[a] for a in FSDP)

    def local(inputs, value_weight, threshold, queries, keys, out_grad):
        tok_rows = queries.shape[0]
        hop_count = WINDOW // TOK_DEV
        span_keys = (hop_count + 1) * tok_rows
        head_ratio = Q_HEADS // KV_HEADS
        kv_pair = 2
        group_count = KV_HEADS // kv_pair
        position = lax.axis_index(ALL)
        earlier = [passed_along(keys, ALL, n_all, distance) for distance in range(hop_count, 0, -1)]
        key_rows = jnp.concatenate(earlier + [keys], axis=0)
        query_pos = position * tok_rows + jnp.arange(tok_rows, dtype=jnp.int32)
        key_pos = (position - hop_count) * tok_rows + jnp.arange(span_keys, dtype=jnp.int32)
        offset = query_pos[:, None] - key_pos[None, :]
        visible = (offset >= 0) & (offset < WINDOW) & (key_pos >= 0)[None, :]
        q_span = kv_pair * head_ratio * HEAD
        k_span = kv_pair * HEAD

        value_parts = []
        for group_index in range(group_count):
            q_cols = queries[:, group_index * q_span : (group_index + 1) * q_span].reshape(
                tok_rows, kv_pair, head_ratio, HEAD
            )
            d_cols = out_grad[:, group_index * q_span : (group_index + 1) * q_span].reshape(
                tok_rows, kv_pair, head_ratio, HEAD
            )
            k_cols = key_rows[:, group_index * k_span : (group_index + 1) * k_span].reshape(
                span_keys, kv_pair, HEAD
            )
            scores = (
                jnp.einsum("qgrd,kgd->grqk", q_cols, k_cols, preferred_element_type=jnp.float32)
                * pre_scale
            )
            scores = jnp.where(visible, scores, masked_score)
            row_max = jnp.max(scores, axis=-1, keepdims=True)
            weights = jnp.exp(scores - row_max)
            probabilities = (weights / jnp.sum(weights, axis=-1, keepdims=True)).astype(jnp.bfloat16)
            value_part = jnp.einsum(
                "grqk,qgrd->kgd", probabilities, d_cols, preferred_element_type=jnp.float32
            )
            value_parts.append(value_part.reshape(span_keys, k_span))

        partial_grad = jnp.concatenate(value_parts, axis=1)

        def block_at(distance):
            return partial_grad[
                (hop_count - distance) * tok_rows : (hop_count - distance + 1) * tok_rows
            ]

        own_grad = block_at(0)
        for distance in range(1, hop_count + 1):
            sent = passed_along(block_at(distance).astype(jnp.bfloat16), ALL, n_all, -distance)
            own_grad = own_grad + sent.astype(jnp.float32)
        value_grad = own_grad.astype(jnp.bfloat16)

        spread = jnp.broadcast_to(value_grad[None], (n_fsdp,) + value_grad.shape)
        gathered = lax.all_to_all(spread, FSDP, 0, 0, tiled=True).reshape(
            n_fsdp * tok_rows, value_grad.shape[1]
        )
        local_grad = jnp.dot(inputs, gathered, preferred_element_type=jnp.float32)

        weight_full = value_weight.astype(jnp.float32)
        kept_mask = jnp.abs(weight_full) > threshold[None, :]
        signed = jnp.where(kept_mask, jnp.sign(weight_full), 0.0)

        logit_part = jnp.sum(local_grad * signed, axis=0)

        rows, cols = local_grad.shape
        n_z = lax.axis_size("z")
        half = cols // 2
        piece = half // n_z
        xh_index = lax.axis_index("xh")
        keep = lax.dynamic_slice_in_dim(local_grad, xh_index * half, half, 1)
        send = lax.dynamic_slice_in_dim(local_grad, (1 - xh_index) * half, half, 1)
        swapped = keep + lax.ppermute(send, "xh", [(0, 1), (1, 0)])
        for axis in ("c", "xl", "y"):
            logit_part = lax.psum(logit_part, axis)
        logit_keep = lax.dynamic_slice_in_dim(logit_part, xh_index * half, half, 0)
        logit_other = lax.dynamic_slice_in_dim(logit_part, (1 - xh_index) * half, half, 0)
        payload = jnp.concatenate([swapped, logit_keep[None], logit_other[None]], axis=0)
        received = lax.all_to_all(payload.reshape(rows + 2, n_z, piece), "z", 1, 1, tiled=True)
        summed = jnp.sum(received, axis=1)
        dense_piece = summed[:rows]
        logit_piece = summed[rows:]
        z_index = lax.axis_index("z")
        kept_piece = lax.dynamic_slice_in_dim(
            kept_mask, xh_index * half + z_index * piece, piece, 1
        )
        weight_piece = jnp.where(kept_piece, dense_piece, 0.0).astype(jnp.bfloat16)
        logit_hi = logit_piece.astype(jnp.bfloat16)
        logit_lo = (logit_piece - logit_hi.astype(jnp.float32)).astype(jnp.bfloat16)
        out_piece = jnp.concatenate(
            [weight_piece, logit_hi[:1], logit_lo[:1], logit_hi[1:], logit_lo[1:]], axis=0
        )
        out_piece = lax.all_gather(out_piece, "z", axis=1, tiled=True)
        out_full = lax.all_gather(out_piece, "xh", axis=1, tiled=True)
        grad_weight = out_full[:rows]
        logit_wide = out_full[rows:].astype(jnp.float32)
        logit_own = logit_wide[0] + logit_wide[1]
        logit_oth = logit_wide[2] + logit_wide[3]
        logit_sum = logit_own + jnp.concatenate([logit_oth[half:], logit_oth[:half]], axis=0)
        grad_logit = -logit_sum * threshold * (1.0 - threshold)
        return (grad_weight, grad_logit)

    return local


def solution(mesh):
    names = mesh.axis_names
    assert tuple(names) == ("seq", "fsdp")
    n_seq, n_fsdp = mesh.devices.shape
    sizes = {"z": n_seq // 2, "xh": 2, "y": n_fsdp // 4, "xl": 2, "c": 2}
    phys = Mesh(
        mesh.devices.reshape([sizes[a] for a in ALL]), ALL
    )
    return jax.shard_map(
        make_local(sizes),
        mesh=phys,
        in_specs=(
            P(FSDP, SEQ),
            P(FSDP, None),
            P(),
            P(ALL, None),
            P(ALL, None),
            P(ALL, None),
        ),
        out_specs=(P(FSDP, None), P()),
        check_vma=False,
    )
```
